256 devices in a mesh: dp: 32 (over x, y, z_lo), tensor: 8 (over z_hi, core).
Axes of the slice: x: 4, y: 4, z: 8 (z_hi: 4, z_lo: 2; z = z_hi * 2 + z_lo), core: 2. Of those that a mesh axis runs over, the one named last changes fastest.
Arguments:
- arrivals: bfloat16 [32768, 2048], P('dp', 'tensor')
- deal: int32 [32, 32], P('dp'), may hold values from 0 to 1023, as said below
- seg_ids: int32 [32, 1024], P('dp'), may hold values from 0 to 7, never falling along the last dimension, each value on 1 to 512 neighbouring positions
- page_table: int32 [32, 8], P('dp'), may hold values from 0 to 7, each once within a row
- attn_gain: float32 [2048], replicated, may hold values from 0.1 to 1.9
- w_query: bfloat16 [2048, 1024], P(None, 'tensor'), may hold values from -0.125 to 0.125
- w_keyval: bfloat16 [2048, 512], replicated, may hold values from -0.125 to 0.125
- query_gain: float32 [64], replicated, may hold values from 0.1 to 1.9
- key_gain: float32 [64], replicated, may hold values from 0.1 to 1.9
- w_out: bfloat16 [1024, 2048], P('tensor'), may hold values from -0.1875 to 0.1875
- ffn_gain: float32 [2048], replicated, may hold values from 0.1 to 1.9
- w_gate: bfloat16 [2048, 5120], P(None, 'tensor'), may hold values from -0.125 to 0.125
- w_up: bfloat16 [2048, 5120], P(None, 'tensor'), may hold values from -0.125 to 0.125
- w_down: bfloat16 [5120, 2048], P('tensor'), may hold values from -0.078125 to 0.078125
Outputs:
- result: bfloat16 [32768, 2048], P('dp', 'tensor')
- kv_pages: bfloat16 [256, 128, 512], P('dp', None, 'tensor')
The draws below stay inside these ranges and needn't reach their ends.
Inputs may be any that keep to these rules, and one draw needn't show every extreme that they name: deal[s, k] = g * 32 + j sends unit k of arrival block s to unit j of group g; every value occurs once; the units of one arrival block go to exactly 16 groups, 2 units to each. `seg_ids`: each row never falls; one prompt is one run of equal numbers. `page_table`: each row holds every page number once.
All inputs are finite; a program needn't handle non-finite values.
Results may differ from the reference program's by a relative error of at most 0.019.
Values may be sent and summed in bfloat16 or wider, within the bound.
No kernel may reach another device: no remote copies, remote signals or barrier semaphores. Data moves between devices by JAX's collectives and lax.ppermute only.
A program may use at most 128 MiB of HBM per device.

```python
import math
import jax
import jax.numpy as jnp
import numpy as np
from jax import lax

D = 2048
HEAD = 64
QH = 16
KVH = 4
FF = 5120
TOK_GRP = 1024
UNITS = 32
MOST = 2
PAGE = 128
SEGS = 8
UNIT = 32
PAGES = 8
GROUPS = 32
TOKENS = 32768
N_TENSOR = 8


def draw_arrivals(key, part):
    keys = jax.random.split(jax.random.fold_in(key, 3), 3)
    row_scale = jnp.exp(jax.random.uniform(keys[0], (TOKENS, 1), jnp.float32, math.log(0.5), math.log(1.5)))
    col_scale = jnp.exp(jax.random.uniform(keys[1], (1, D), jnp.float32, math.log(0.3), math.log(1.5)))
    base = jnp.clip(jax.random.normal(keys[2], (TOKENS, D), jnp.float32), -3.5, 3.5)
    return (base * row_scale * col_scale).astype(jnp.bfloat16)


def permute_units(key):
    return jax.random.permutation(key, UNITS)


def draw_deal(key, part):
    keys = jax.random.split(jax.random.fold_in(key, 7), 4)
    pairs = UNITS // MOST
    offsets = jax.random.permutation(keys[0], GROUPS)[:pairs]
    owners = jax.random.permutation(keys[1], GROUPS)
    orders = jax.vmap(permute_units)(jax.random.split(keys[2], GROUPS))
    places = jax.vmap(permute_units)(jax.random.split(keys[3], GROUPS))
    source = jnp.arange(GROUPS, dtype=jnp.int32)[:, None]
    target = owners[(source + offsets[orders // MOST]) % GROUPS]
    place = places[target, orders]
    return (target * UNITS + place).astype(jnp.int32)


def level_of(rng, dims, cuts, least, high):
    level = 1.0
    for dim, parts in cuts:
        steps = jax.random.uniform(jax.random.fold_in(jax.random.fold_in(rng, 6), dim), (parts,), jnp.float32, least / len(cuts), high / len(cuts))
        level = level * jnp.repeat(jnp.exp(steps), dims[dim] // parts).reshape((-1,) + (1,) * (len(dims) - 1 - dim))
    return level


def profile(number_of, total, limit, slope):
    weights = [(1 << 20) // math.isqrt(standing ** slope) + 1 for standing in range(2, number_of + 1)]
    spare, given = total - limit - (number_of - 1), [1] * (number_of - 1)
    while spare > 0:
        free = [i for i in range(number_of - 1) if given[i] < limit]
        mass, remaining = sum([weights[i] for i in free]), spare
        for i in free:
            more = min(limit - given[i], max(1, remaining * weights[i] // mass), spare)
            given[i] = given[i] + more
            spare = spare - more
    return np.array([limit] + given)


def uneven_parts(rng, count, total, limit, lean):
    if count == 2:
        one = jax.random.randint(rng, (), max(1, total - limit), min(limit, total - 1) + 1)
        return jnp.stack([one, total - one])
    tallies = jnp.asarray(profile(count, total, limit, lean), jnp.int32)
    twos = (count - 1) // 2
    giver, sink = tallies[1:1 + 2 * twos:2], tallies[2:2 + 2 * twos:2]
    slack = jnp.minimum(giver - 1, limit - sink)
    shifted = jax.random.randint(jax.random.fold_in(rng, 1), (twos,), 0, 1 << 20) % (slack + 1)
    tallies = tallies.at[1:1 + 2 * twos:2].set(giver - shifted).at[2:2 + 2 * twos:2].set(sink + shifted)
    return tallies[jax.random.permutation(jax.random.fold_in(rng, 2), count)]


def scatter_about(own_key, extent, scale, reach, cuts=(), kind=jnp.bfloat16):
    array = jax.random.normal(own_key, extent, jnp.float32) * scale
    if len(cuts) > 0:
        array = level_of(own_key, extent, cuts, -0.22, 0.18) * array
    return jnp.clip(array, min=-reach, max=reach).astype(kind)


def setup_inputs(seed: int = 0) -> dict:
    arg_keys = jax.random.split(jax.random.key(seed), 15)
    arrivals = draw_arrivals(jax.random.fold_in(arg_keys[14], 71), 0)
    deal = draw_deal(jax.random.fold_in(arg_keys[14], 71), 0)
    seg_ids = jax.vmap(lambda own: jnp.searchsorted(jnp.cumsum(uneven_parts(own, SEGS, TOK_GRP, TOK_GRP // 2, 2)), jnp.arange(TOK_GRP), side="right"))(jax.random.split(arg_keys[2], GROUPS)).reshape((GROUPS, TOK_GRP)).astype(jnp.int32)
    page_table = jax.vmap(lambda own: jax.random.permutation(own, PAGES))(jax.random.split(arg_keys[3], GROUPS)).reshape((GROUPS, PAGES)).astype(jnp.int32)
    attn_gain = jnp.clip(1.0 + 0.18 * jax.random.normal(arg_keys[4], (D,), jnp.float32), 0.1, 1.9)
    w_query = scatter_about(arg_keys[5], (D, QH * HEAD), D ** -0.5, 0.125, ((1, 8),))
    w_keyval = scatter_about(arg_keys[6], (D, 2 * KVH * HEAD), D ** -0.5, 0.125)
    query_gain = jnp.clip(1.0 + 0.18 * jax.random.normal(arg_keys[7], (HEAD,), jnp.float32), 0.1, 1.9)
    key_gain = jnp.clip(1.0 + 0.18 * jax.random.normal(arg_keys[8], (HEAD,), jnp.float32), 0.1, 1.9)
    w_out = scatter_about(arg_keys[9], (QH * HEAD, D), (QH * HEAD) ** -0.5, 0.1875, ((0, 8),))
    ffn_gain = jnp.clip(1.0 + 0.18 * jax.random.normal(arg_keys[10], (D,), jnp.float32), 0.1, 1.9)
    w_gate = scatter_about(arg_keys[11], (D, FF), D ** -0.5, 0.125, ((1, 8),))
    w_up = scatter_about(arg_keys[12], (D, FF), D ** -0.5, 0.125, ((1, 8),))
    w_down = scatter_about(arg_keys[13], (FF, D), FF ** -0.5, 0.078125, ((0, 8),))
    return dict(arrivals=arrivals, deal=deal, seg_ids=seg_ids, page_table=page_table, attn_gain=attn_gain, w_query=w_query, w_keyval=w_keyval, query_gain=query_gain, key_gain=key_gain, w_out=w_out, ffn_gain=ffn_gain, w_gate=w_gate, w_up=w_up, w_down=w_down)


EPS = 1e-06
THETA = 10000.0

def rms_scale(values, gain):
    values = values.astype(jnp.float32)
    mean_sq = lax.optimization_barrier(jnp.mean(values * values, axis=-1, keepdims=True))
    return values * lax.rsqrt(mean_sq + EPS) * gain.astype(jnp.float32)

def rope_tables(positions, width):
    half = width // 2
    inverse = THETA ** (-jnp.arange(half, dtype=jnp.float32) * 2.0 / width)
    angles = positions.astype(jnp.float32)[:, None] * inverse[None, :]
    return (jnp.cos(angles), jnp.sin(angles))

def rotate(values, cosine, sine):
    half = values.shape[-1] // 2
    first = values[..., :half]
    second = values[..., half:]
    cos_b = cosine[:, None, :]
    sin_b = sine[:, None, :]
    return jnp.concatenate([first * cos_b - second * sin_b, second * cos_b + first * sin_b], axis=-1)

def segment_starts(seg_row):
    count = seg_row.shape[0]
    index = jnp.arange(count, dtype=jnp.int32)
    prior = jnp.concatenate([seg_row[:1] - 1, seg_row[:-1]])
    marks = jnp.where(seg_row != prior, index, 0).astype(jnp.int32)
    return lax.cummax(marks, axis=0)

def partial_sum(left, right, blocks):
    width = left.shape[1] // blocks
    total = jnp.zeros((left.shape[0], right.shape[1]), jnp.float32)
    for block in range(blocks):
        term = jnp.dot(left[:, block * width:(block + 1) * width], right[block * width:(block + 1) * width], preferred_element_type=jnp.float32).astype(jnp.bfloat16)
        term = lax.optimization_barrier(term)
        total = total + term.astype(jnp.float32)
    return total

def reference(arrivals, deal, seg_ids, page_table, attn_gain, w_query, w_keyval, query_gain, key_gain, w_out, ffn_gain, w_gate, w_up, w_down):
    units_all = arrivals.reshape(GROUPS * UNITS, UNIT, D)
    slots = deal.reshape(-1).astype(jnp.int32)
    grouped = jnp.zeros_like(units_all).at[slots].set(units_all).reshape(GROUPS, TOK_GRP, D)

    def one_group(inputs):
        rows, seg_row, table = inputs
        normed = rms_scale(rows, attn_gain).astype(jnp.bfloat16)
        starts = segment_starts(seg_row)
        index = jnp.arange(TOK_GRP, dtype=jnp.int32)
        cosine, sine = rope_tables(index - starts, HEAD)
        q_raw = jnp.dot(normed, w_query, preferred_element_type=jnp.float32).reshape(TOK_GRP, QH, HEAD)
        queries = rotate(rms_scale(q_raw, query_gain), cosine, sine).astype(jnp.bfloat16)
        kv_raw = jnp.dot(normed, w_keyval, preferred_element_type=jnp.float32).reshape(TOK_GRP, KVH, 2, HEAD)
        keys = rotate(rms_scale(kv_raw[:, :, 0], key_gain), cosine, sine).astype(jnp.bfloat16)
        values = kv_raw[:, :, 1].astype(jnp.bfloat16)
        cache = jnp.stack([keys, values], axis=2).reshape(PAGES, PAGE, KVH * 2 * HEAD)
        cache = jnp.zeros_like(cache).at[table.astype(jnp.int32)].set(cache)
        q_grouped = queries.astype(jnp.float32).reshape(TOK_GRP, KVH, QH // KVH, HEAD)
        scores = jnp.einsum('ikgd,jkd->kgij', q_grouped, keys.astype(jnp.float32)) * (1.0 / math.sqrt(HEAD))
        allowed = jnp.logical_and(index[:, None] >= index[None, :], starts[:, None] <= index[None, :])
        weights = jnp.where(allowed, jnp.exp(scores), 0.0)
        probs = (weights / lax.optimization_barrier(jnp.sum(weights, axis=-1, keepdims=True))).astype(jnp.bfloat16)
        attended = jnp.einsum('kgij,jkd->ikgd', probs.astype(jnp.float32), values.astype(jnp.float32))
        attended = attended.astype(jnp.bfloat16).reshape(TOK_GRP, QH * HEAD)
        middle = (rows.astype(jnp.float32) + partial_sum(attended, w_out, N_TENSOR)).astype(jnp.bfloat16)
        ffn_in = rms_scale(middle, ffn_gain).astype(jnp.bfloat16)
        gate = jnp.dot(ffn_in, w_gate, preferred_element_type=jnp.float32)
        upper = jnp.dot(ffn_in, w_up, preferred_element_type=jnp.float32)
        hidden = (jax.nn.silu(gate) * upper).astype(jnp.bfloat16)
        combined = (middle.astype(jnp.float32) + partial_sum(hidden, w_down, N_TENSOR)).astype(jnp.bfloat16)
        return (combined, cache)
    combined, caches = lax.map(one_group, (grouped, seg_ids, page_table))
    back = combined.reshape(GROUPS * UNITS, UNIT, D)[slots]
    return (back.reshape(TOKENS, D), caches.reshape(GROUPS * PAGES, PAGE, KVH * 2 * HEAD))
```

```python
import math

import jax
import jax.numpy as jnp
from jax import lax
from jax.sharding import PartitionSpec as P

HEAD = 64
KVH = 4
MOST = 2
PAGE = 128


EPS = 1e-06
THETA = 10000.0
BLOCK_ROWS = 512


def rms_scale(values, gain):
    values = values.astype(jnp.float32)
    mean_sq = jnp.mean(values * values, axis=-1, keepdims=True)
    return values * lax.rsqrt(mean_sq + EPS) * gain


def rope_tables(positions, width):
    half = width // 2
    inverse = THETA ** (-jnp.arange(half, dtype=jnp.float32) * 2.0 / width)
    angles = positions.astype(jnp.float32)[:, None] * inverse[None, :]
    return (jnp.cos(angles), jnp.sin(angles))


def rotate(values, cosine, sine):
    half = values.shape[-1] // 2
    first = values[..., :half]
    second = values[..., half:]
    cos_b = cosine[:, None, :]
    sin_b = sine[:, None, :]
    return jnp.concatenate(
        [first * cos_b - second * sin_b, second * cos_b + first * sin_b], axis=-1
    )


def segment_starts(seg_row):
    count = seg_row.shape[0]
    index = jnp.arange(count, dtype=jnp.int32)
    prior = jnp.concatenate([seg_row[:1] - 1, seg_row[:-1]])
    marks = jnp.where(seg_row != prior, index, 0)
    return lax.cummax(marks, axis=0)


def on_device(
    arrivals,
    deal,
    seg_ids,
    page_table,
    attn_gain,
    w_query,
    w_keyval,
    query_gain,
    key_gain,
    w_out,
    ffn_gain,
    w_gate,
    w_up,
    w_down,
):
    groups = lax.axis_size("dp")
    shards = lax.axis_size("tensor")
    tensor_rank = lax.axis_index("tensor")
    tok_grp = arrivals.shape[0]
    feat_part = arrivals.shape[1]
    units = deal.shape[1]
    unit_rows = tok_grp // units
    slot_count = groups * MOST
    width = unit_rows * feat_part
    dest_row = deal[0]
    target = dest_row // units
    position = dest_row % units
    unit_index = jnp.arange(units, dtype=jnp.int32)
    earlier = unit_index[:, None] > unit_index[None, :]
    same_target = target[:, None] == target[None, :]
    rank = jnp.sum(jnp.logical_and(earlier, same_target), axis=1)
    slot = target * MOST + rank
    send_hot = slot[None, :] == jnp.arange(slot_count, dtype=jnp.int32)[:, None]
    filled = jnp.any(send_hot, axis=1)
    slot_pos = jnp.where(filled, jnp.sum(jnp.where(send_hot, position[None, :], 0), axis=1), -1)
    send_matrix = send_hot.astype(jnp.bfloat16)
    w_out_full = lax.all_gather(w_out, "tensor", axis=0, tiled=True)
    packed = jnp.dot(
        send_matrix, arrivals.reshape(units, width), preferred_element_type=jnp.float32
    ).astype(jnp.bfloat16)
    pos_cols = jnp.broadcast_to(slot_pos.astype(jnp.bfloat16)[:, None], (slot_count, 128))
    packed = jnp.concatenate([packed, pos_cols], axis=1)
    received = lax.all_to_all(
        packed.reshape(groups, MOST, width + 128), "dp", split_axis=0, concat_axis=0, tiled=True
    ).reshape(slot_count, width + 128)
    recv_pos = received[:, width].astype(jnp.int32)
    recv_matrix = (recv_pos[None, :] == unit_index[:, None]).astype(jnp.bfloat16)
    grouped = jnp.dot(
        recv_matrix, received[:, :width], preferred_element_type=jnp.float32
    ).astype(jnp.bfloat16)
    grouped = grouped.reshape(tok_grp, feat_part)
    grouped, w_out_full = lax.optimization_barrier((grouped, w_out_full))
    full = lax.all_gather(grouped, "tensor", axis=1, tiled=True)
    normed = rms_scale(full, attn_gain).astype(jnp.bfloat16)
    seg_row = seg_ids[0]
    starts = segment_starts(seg_row)
    index = jnp.arange(tok_grp, dtype=jnp.int32)
    cosine, sine = rope_tables(index - starts, HEAD)
    q_heads = w_query.shape[1] // HEAD
    q_raw = jnp.dot(normed, w_query, preferred_element_type=jnp.float32).reshape(
        tok_grp, q_heads, HEAD
    )
    queries = rotate(rms_scale(q_raw, query_gain), cosine, sine).astype(jnp.bfloat16)
    kv_heads = max(1, KVH // shards)
    kv_first = tensor_rank * KVH // shards
    kv_weight = lax.dynamic_slice_in_dim(w_keyval, kv_first * 2 * HEAD, kv_heads * 2 * HEAD, 1)
    kv_raw = jnp.dot(normed, kv_weight, preferred_element_type=jnp.float32).reshape(
        tok_grp, kv_heads, 2, HEAD
    )
    keys = rotate(rms_scale(kv_raw[:, :, 0], key_gain), cosine, sine).astype(jnp.bfloat16)
    values = kv_raw[:, :, 1].astype(jnp.bfloat16)
    stacked = jnp.stack([keys, values], axis=2).reshape(tok_grp, kv_heads * 2 * HEAD)
    cache_cols = 2 * KVH * HEAD // shards
    offset = tensor_rank * cache_cols - kv_first * 2 * HEAD
    own_cache = lax.dynamic_slice_in_dim(stacked, offset, cache_cols, 1)
    pages = own_cache.reshape(tok_grp // PAGE, PAGE, cache_cols)
    kv_pages = jnp.zeros_like(pages).at[page_table[0]].set(pages)
    share = q_heads // kv_heads
    grouped_q = queries.reshape(tok_grp, kv_heads, share, HEAD)
    scale = 1.0 / math.sqrt(HEAD)
    block = min(BLOCK_ROWS, tok_grp)
    outputs = []
    for first in range(0, tok_grp, block):
        last = first + block
        scores = (
            jnp.einsum(
                "ikgd,jkd->kgij",
                grouped_q[first:last],
                keys[:last],
                preferred_element_type=jnp.float32,
            )
            * scale
        )
        query_rows = index[first:last]
        allowed = jnp.logical_and(
            query_rows[:, None] >= index[None, :last],
            starts[first:last][:, None] <= index[None, :last],
        )
        weights = jnp.where(allowed, jnp.exp(scores), 0.0)
        probs = (weights / jnp.sum(weights, axis=-1, keepdims=True)).astype(jnp.bfloat16)
        mixed = jnp.einsum(
            "kgij,jkd->ikgd", probs, values[:last], preferred_element_type=jnp.float32
        )
        outputs.append(mixed.astype(jnp.bfloat16).reshape(block, q_heads * HEAD))
    attended = jnp.concatenate(outputs, axis=0)
    attended_full = lax.all_gather(attended, "tensor", axis=1, tiled=True)
    attn_sum = jnp.dot(attended_full, w_out_full, preferred_element_type=jnp.float32)
    middle = (full.astype(jnp.float32) + attn_sum).astype(jnp.bfloat16)
    ffn_in = rms_scale(middle, ffn_gain).astype(jnp.bfloat16)
    gate = jnp.dot(ffn_in, w_gate, preferred_element_type=jnp.float32)
    upper = jnp.dot(ffn_in, w_up, preferred_element_type=jnp.float32)
    hidden = (jax.nn.silu(gate) * upper).astype(jnp.bfloat16)
    ffn_part = lax.psum_scatter(
        jnp.dot(hidden, w_down, preferred_element_type=jnp.float32).astype(jnp.bfloat16),
        "tensor",
        scatter_dimension=1,
        tiled=True,
    ).astype(jnp.float32)
    own_cols = lax.dynamic_slice_in_dim(middle, tensor_rank * feat_part, feat_part, 1)
    combined = (own_cols.astype(jnp.float32) + ffn_part).astype(jnp.bfloat16)
    back = jnp.dot(
        recv_matrix.T, combined.reshape(units, width), preferred_element_type=jnp.float32
    ).astype(jnp.bfloat16)
    returned = lax.all_to_all(
        back.reshape(groups, MOST, width), "dp", split_axis=0, concat_axis=0, tiled=True
    )
    result = jnp.dot(
        send_matrix.T, returned.reshape(slot_count, width), preferred_element_type=jnp.float32
    ).astype(jnp.bfloat16)
    return (result.reshape(tok_grp, feat_part), kv_pages)


def solution(mesh):
    return jax.shard_map(
        on_device,
        mesh=mesh,
        in_specs=(
            P("dp", "tensor"),
            P("dp", None),
            P("dp", None),
            P("dp", None),
            P(),
            P(None, "tensor"),
            P(),
            P(),
            P(),
            P("tensor", None),
            P(),
            P(None, "tensor"),
            P(None, "tensor"),
            P("tensor", None),
        ),
        out_specs=(P("dp", "tensor"), P("dp", None, "tensor")),
        check_vma=False,
    )
```

```python
import math

import jax
import jax.numpy as jnp
from jax import lax
from jax.sharding import PartitionSpec as P

HEAD = 64
KVH = 4
MOST = 2
PAGE = 128


EPS = 1e-06
THETA = 10000.0
BLOCK_ROWS = 512


def rms_scale(values, gain):
    values = values.astype(jnp.float32)
    mean_sq = jnp.mean(values * values, axis=-1, keepdims=True)
    return values * lax.rsqrt(mean_sq + EPS) * gain


def rope_tables(positions, width):
    half = width // 2
    inverse = THETA ** (-jnp.arange(half, dtype=jnp.float32) * 2.0 / width)
    angles = positions.astype(jnp.float32)[:, None] * inverse[None, :]
    return (jnp.cos(angles), jnp.sin(angles))


def rotate(values, cosine, sine):
    half = values.shape[-1] // 2
    first = values[..., :half]
    second = values[..., half:]
    cos_b = cosine[:, None, :]
    sin_b = sine[:, None, :]
    return jnp.concatenate(
        [first * cos_b - second * sin_b, second * cos_b + first * sin_b], axis=-1
    )


def segment_starts(seg_row):
    count = seg_row.shape[0]
    index = jnp.arange(count, dtype=jnp.int32)
    prior = jnp.concatenate([seg_row[:1] - 1, seg_row[:-1]])
    marks = jnp.where(seg_row != prior, index, 0)
    return lax.cummax(marks, axis=0)


def on_device(
    arrivals,
    deal,
    seg_ids,
    page_table,
    attn_gain,
    w_query,
    w_keyval,
    query_gain,
    key_gain,
    w_out,
    ffn_gain,
    w_gate,
    w_up,
    w_down,
):
    groups = lax.axis_size("dp")
    shards = lax.axis_size("tensor")
    tensor_rank = lax.axis_index("tensor")
    tok_grp = arrivals.shape[0]
    feat_part = arrivals.shape[1]
    units = deal.shape[1]
    unit_rows = tok_grp // units
    slot_count = groups * MOST
    width = unit_rows * feat_part
    dest_row = deal[0]
    target = dest_row // units
    unit_index = jnp.arange(units, dtype=jnp.int32)
    earlier = unit_index[:, None] > unit_index[None, :]
    same_target = target[:, None] == target[None, :]
    rank = jnp.sum(jnp.logical_and(earlier, same_target), axis=1)
    slot = target * MOST + rank
    slot_index = jnp.arange(slot_count, dtype=jnp.int32)
    send_hot = slot[None, :] == slot_index[:, None]
    send_src = jnp.sum(jnp.where(send_hot, unit_index[None, :], 0), axis=1)
    w_out_full = lax.all_gather(w_out, "tensor", axis=0, tiled=True)
    deal_all = lax.all_gather(deal, "dp", axis=0, tiled=True)
    own_group = lax.axis_index("dp")
    tgt_all = deal_all // units
    same_all = tgt_all[:, :, None] == tgt_all[:, None, :]
    rank_all = jnp.sum(jnp.logical_and(earlier[None], same_all), axis=2)
    slot_all = jnp.arange(groups, dtype=jnp.int32)[:, None] * MOST + rank_all
    mine = tgt_all == own_group
    pos_all = deal_all % units
    pos_hot = jnp.logical_and(mine[None], pos_all[None] == unit_index[:, None, None])
    slot_of_pos = jnp.sum(jnp.where(pos_hot, slot_all[None], 0), axis=(1, 2))
    back_hot = jnp.logical_and(mine[None], slot_all[None] == slot_index[:, None, None])
    pos_of_slot = jnp.sum(jnp.where(back_hot, pos_all[None], 0), axis=(1, 2))
    arrival_units = arrivals.reshape(units, unit_rows, feat_part)
    packed = jnp.take(arrival_units, send_src, axis=0, mode="clip")
    received = lax.all_to_all(
        packed.reshape(groups, MOST, unit_rows, feat_part), "dp", split_axis=0, concat_axis=0, tiled=True
    ).reshape(slot_count, unit_rows, feat_part)
    grouped = jnp.take(received, slot_of_pos, axis=0, mode="clip")
    grouped = grouped.reshape(tok_grp, feat_part)
    grouped, w_out_full = lax.optimization_barrier((grouped, w_out_full))
    full = lax.all_gather(grouped, "tensor", axis=1, tiled=True)
    normed = rms_scale(full, attn_gain).astype(jnp.bfloat16)
    seg_row = seg_ids[0]
    starts = segment_starts(seg_row)
    index = jnp.arange(tok_grp, dtype=jnp.int32)
    cosine, sine = rope_tables(index - starts, HEAD)
    q_heads = w_query.shape[1] // HEAD
    q_raw = jnp.dot(normed, w_query, preferred_element_type=jnp.float32).reshape(
        tok_grp, q_heads, HEAD
    )
    queries = rotate(rms_scale(q_raw, query_gain), cosine, sine).astype(jnp.bfloat16)
    kv_heads = max(1, KVH // shards)
    kv_first = tensor_rank * KVH // shards
    kv_weight = lax.dynamic_slice_in_dim(w_keyval, kv_first * 2 * HEAD, kv_heads * 2 * HEAD, 1)
    kv_raw = jnp.dot(normed, kv_weight, preferred_element_type=jnp.float32).reshape(
        tok_grp, kv_heads, 2, HEAD
    )
    keys = rotate(rms_scale(kv_raw[:, :, 0], key_gain), cosine, sine).astype(jnp.bfloat16)
    values = kv_raw[:, :, 1].astype(jnp.bfloat16)
    stacked = jnp.stack([keys, values], axis=2).reshape(tok_grp, kv_heads * 2 * HEAD)
    cache_cols = 2 * KVH * HEAD // shards
    offset = tensor_rank * cache_cols - kv_first * 2 * HEAD
    own_cache = lax.dynamic_slice_in_dim(stacked, offset, cache_cols, 1)
    pages = own_cache.reshape(tok_grp // PAGE, PAGE, cache_cols)
    kv_pages = jnp.zeros_like(pages).at[page_table[0]].set(pages)
    share = q_heads // kv_heads
    grouped_q = queries.reshape(tok_grp, kv_heads, share, HEAD)
    scale = 1.0 / math.sqrt(HEAD)
    block = min(BLOCK_ROWS, tok_grp)
    outputs = []
    for first in range(0, tok_grp, block):
        last = first + block
        scores = (
            jnp.einsum(
                "ikgd,jkd->kgij",
                grouped_q[first:last],
                keys[:last],
                preferred_element_type=jnp.float32,
            )
            * scale
        )
        query_rows = index[first:last]
        allowed = jnp.logical_and(
            query_rows[:, None] >= index[None, :last],
            starts[first:last][:, None] <= index[None, :last],
        )
        weights = jnp.where(allowed, jnp.exp(scores), 0.0)
        probs = (weights / jnp.sum(weights, axis=-1, keepdims=True)).astype(jnp.bfloat16)
        mixed = jnp.einsum(
            "kgij,jkd->ikgd", probs, values[:last], preferred_element_type=jnp.float32
        )
        outputs.append(mixed.astype(jnp.bfloat16).reshape(block, q_heads * HEAD))
    attended = jnp.concatenate(outputs, axis=0)
    attended_full = lax.all_gather(attended, "tensor", axis=1, tiled=True)
    attn_sum = jnp.dot(attended_full, w_out_full, preferred_element_type=jnp.float32)
    middle = (full.astype(jnp.float32) + attn_sum).astype(jnp.bfloat16)
    ffn_in = rms_scale(middle, ffn_gain).astype(jnp.bfloat16)
    gate = jnp.dot(ffn_in, w_gate, preferred_element_type=jnp.float32)
    upper = jnp.dot(ffn_in, w_up, preferred_element_type=jnp.float32)
    hidden = (jax.nn.silu(gate) * upper).astype(jnp.bfloat16)
    ffn_part = lax.psum_scatter(
        jnp.dot(hidden, w_down, preferred_element_type=jnp.float32).astype(jnp.bfloat16),
        "tensor",
        scatter_dimension=1,
        tiled=True,
    ).astype(jnp.float32)
    own_cols = lax.dynamic_slice_in_dim(middle, tensor_rank * feat_part, feat_part, 1)
    combined = (own_cols.astype(jnp.float32) + ffn_part).astype(jnp.bfloat16)
    back = jnp.take(combined.reshape(units, unit_rows, feat_part), pos_of_slot, axis=0, mode="clip")
    returned = lax.all_to_all(
        back.reshape(groups, MOST, unit_rows, feat_part), "dp", split_axis=0, concat_axis=0, tiled=True
    ).reshape(slot_count, unit_rows, feat_part)
    result = jnp.take(returned, slot, axis=0, mode="clip")
    return (result.reshape(tok_grp, feat_part), kv_pages)


def solution(mesh):
    return jax.shard_map(
        on_device,
        mesh=mesh,
        in_specs=(
            P("dp", "tensor"),
            P("dp", None),
            P("dp", None),
            P("dp", None),
            P(),
            P(None, "tensor"),
            P(),
            P(),
            P(),
            P("tensor", None),
            P(),
            P(None, "tensor"),
            P(None, "tensor"),
            P("tensor", None),
        ),
        out_specs=(P("dp", "tensor"), P("dp", None, "tensor")),
        check_vma=False,
    )
```

```python
import math

import jax
import jax.numpy as jnp
from jax import lax
from jax.sharding import PartitionSpec as P

HEAD = 64
KVH = 4
MOST = 2
PAGE = 128


EPS = 1e-06
THETA = 10000.0
BLOCK_ROWS = 512


def rms_scale(values, gain):
    values = values.astype(jnp.float32)
    mean_sq = jnp.mean(values * values, axis=-1, keepdims=True)
    return values * lax.rsqrt(mean_sq + EPS) * gain


def rope_tables(positions, width):
    half = width // 2
    inverse = THETA ** (-jnp.arange(half, dtype=jnp.float32) * 2.0 / width)
    angles = positions.astype(jnp.float32)[:, None] * inverse[None, :]
    return (jnp.cos(angles), jnp.sin(angles))


def rotate(values, cosine, sine):
    half = values.shape[-1] // 2
    first = values[..., :half]
    second = values[..., half:]
    cos_b = cosine[:, None, :]
    sin_b = sine[:, None, :]
    return jnp.concatenate(
        [first * cos_b - second * sin_b, second * cos_b + first * sin_b], axis=-1
    )


def segment_starts(seg_row):
    count = seg_row.shape[0]
    index = jnp.arange(count, dtype=jnp.int32)
    prior = jnp.concatenate([seg_row[:1] - 1, seg_row[:-1]])
    marks = jnp.where(seg_row != prior, index, 0)
    return lax.cummax(marks, axis=0)


def on_device(
    arrivals,
    deal,
    seg_ids,
    page_table,
    attn_gain,
    w_query,
    w_keyval,
    query_gain,
    key_gain,
    w_out,
    ffn_gain,
    w_gate,
    w_up,
    w_down,
):
    groups = lax.axis_size("dp")
    shards = lax.axis_size("tensor")
    tensor_rank = lax.axis_index("tensor")
    tok_grp = arrivals.shape[0]
    feat_part = arrivals.shape[1]
    units = deal.shape[1]
    unit_rows = tok_grp // units
    slot_count = groups * MOST
    width = unit_rows * feat_part
    dest_row = deal[0]
    target = dest_row // units
    unit_index = jnp.arange(units, dtype=jnp.int32)
    earlier = unit_index[:, None] > unit_index[None, :]
    same_target = target[:, None] == target[None, :]
    rank = jnp.sum(jnp.logical_and(earlier, same_target), axis=1)
    slot = target * MOST + rank
    slot_index = jnp.arange(slot_count, dtype=jnp.int32)
    send_hot = slot[None, :] == slot_index[:, None]
    send_src = jnp.sum(jnp.where(send_hot, unit_index[None, :], 0), axis=1)
    w_out_full = lax.all_gather(w_out, "tensor", axis=0, tiled=True)
    position = dest_row % units
    filled = jnp.any(send_hot, axis=1)
    slot_pos = jnp.where(filled, jnp.sum(jnp.where(send_hot, position[None, :], 0), axis=1), -1)
    pos_block = jnp.zeros((groups, 8, feat_part), jnp.bfloat16)
    pos_block = pos_block.at[:, 0, :MOST].set(slot_pos.reshape(groups, MOST).astype(jnp.bfloat16))
    arrival_units = arrivals.reshape(units, unit_rows, feat_part)
    packed = jnp.take(arrival_units, send_src, axis=0, mode="clip")
    payload = jnp.concatenate(
        [packed.reshape(groups, MOST * unit_rows, feat_part), pos_block], axis=1
    )
    received = lax.all_to_all(payload, "dp", split_axis=0, concat_axis=0, tiled=True)
    recv_pos = received[:, MOST * unit_rows, :MOST].reshape(slot_count).astype(jnp.int32)
    recv_units = received[:, : MOST * unit_rows].reshape(slot_count, unit_rows, feat_part)
    pos_hot = recv_pos[None, :] == unit_index[:, None]
    slot_of_pos = jnp.sum(jnp.where(pos_hot, slot_index[None, :], 0), axis=1)
    pos_of_slot = jnp.maximum(recv_pos, 0)
    grouped = jnp.take(recv_units, slot_of_pos, axis=0, mode="clip")
    grouped = grouped.reshape(tok_grp, feat_part)
    grouped, w_out_full = lax.optimization_barrier((grouped, w_out_full))
    full = lax.all_gather(grouped, "tensor", axis=1, tiled=True)
    normed = rms_scale(full, attn_gain).astype(jnp.bfloat16)
    seg_row = seg_ids[0]
    starts = segment_starts(seg_row)
    index = jnp.arange(tok_grp, dtype=jnp.int32)
    cosine, sine = rope_tables(index - starts, HEAD)
    q_heads = w_query.shape[1] // HEAD
    q_raw = jnp.dot(normed, w_query, preferred_element_type=jnp.float32).reshape(
        tok_grp, q_heads, HEAD
    )
    queries = rotate(rms_scale(q_raw, query_gain), cosine, sine).astype(jnp.bfloat16)
    kv_heads = max(1, KVH // shards)
    kv_first = tensor_rank * KVH // shards
    kv_weight = lax.dynamic_slice_in_dim(w_keyval, kv_first * 2 * HEAD, kv_heads * 2 * HEAD, 1)
    kv_raw = jnp.dot(normed, kv_weight, preferred_element_type=jnp.float32).reshape(
        tok_grp, kv_heads, 2, HEAD
    )
    keys = rotate(rms_scale(kv_raw[:, :, 0], key_gain), cosine, sine).astype(jnp.bfloat16)
    values = kv_raw[:, :, 1].astype(jnp.bfloat16)
    stacked = jnp.stack([keys, values], axis=2).reshape(tok_grp, kv_heads * 2 * HEAD)
    cache_cols = 2 * KVH * HEAD // shards
    offset = tensor_rank * cache_cols - kv_first * 2 * HEAD
    own_cache = lax.dynamic_slice_in_dim(stacked, offset, cache_cols, 1)
    pages = own_cache.reshape(tok_grp // PAGE, PAGE, cache_cols)
    kv_pages = jnp.zeros_like(pages).at[page_table[0]].set(pages)
    share = q_heads // kv_heads
    grouped_q = queries.reshape(tok_grp, kv_heads, share, HEAD)
    scale = 1.0 / math.sqrt(HEAD)
    block = min(BLOCK_ROWS, tok_grp)
    outputs = []
    for first in range(0, tok_grp, block):
        last = first + block
        scores = (
            jnp.einsum(
                "ikgd,jkd->kgij",
                grouped_q[first:last],
                keys[:last],
                preferred_element_type=jnp.float32,
            )
            * scale
        )
        query_rows = index[first:last]
        allowed = jnp.logical_and(
            query_rows[:, None] >= index[None, :last],
            starts[first:last][:, None] <= index[None, :last],
        )
        weights = jnp.where(allowed, jnp.exp(scores), 0.0)
        probs = (weights / jnp.sum(weights, axis=-1, keepdims=True)).astype(jnp.bfloat16)
        mixed = jnp.einsum(
            "kgij,jkd->ikgd", probs, values[:last], preferred_element_type=jnp.float32
        )
        outputs.append(mixed.astype(jnp.bfloat16).reshape(block, q_heads * HEAD))
    attended = jnp.concatenate(outputs, axis=0)
    attended_full = lax.all_gather(attended, "tensor", axis=1, tiled=True)
    attn_sum = jnp.dot(attended_full, w_out_full, preferred_element_type=jnp.float32)
    middle = (full.astype(jnp.float32) + attn_sum).astype(jnp.bfloat16)
    ffn_in = rms_scale(middle, ffn_gain).astype(jnp.bfloat16)
    gate = jnp.dot(ffn_in, w_gate, preferred_element_type=jnp.float32)
    upper = jnp.dot(ffn_in, w_up, preferred_element_type=jnp.float32)
    hidden = (jax.nn.silu(gate) * upper).astype(jnp.bfloat16)
    ffn_part = lax.psum_scatter(
        jnp.dot(hidden, w_down, preferred_element_type=jnp.float32).astype(jnp.bfloat16),
        "tensor",
        scatter_dimension=1,
        tiled=True,
    ).astype(jnp.float32)
    own_cols = lax.dynamic_slice_in_dim(middle, tensor_rank * feat_part, feat_part, 1)
    combined = (own_cols.astype(jnp.float32) + ffn_part).astype(jnp.bfloat16)
    back = jnp.take(combined.reshape(units, unit_rows, feat_part), pos_of_slot, axis=0, mode="clip")
    returned = lax.all_to_all(
        back.reshape(groups, MOST, unit_rows, feat_part), "dp", split_axis=0, concat_axis=0, tiled=True
    ).reshape(slot_count, unit_rows, feat_part)
    result = jnp.take(returned, slot, axis=0, mode="clip")
    return (result.reshape(tok_grp, feat_part), kv_pages)


def solution(mesh):
    return jax.shard_map(
        on_device,
        mesh=mesh,
        in_specs=(
            P("dp", "tensor"),
            P("dp", None),
            P("dp", None),
            P("dp", None),
            P(),
            P(None, "tensor"),
            P(),
            P(),
            P(),
            P("tensor", None),
            P(),
            P(None, "tensor"),
            P(None, "tensor"),
            P("tensor", None),
        ),
        out_specs=(P("dp", "tensor"), P("dp", None, "tensor")),
        check_vma=False,
    )
```

```python
import math

import jax
import jax.numpy as jnp
from jax import lax
from jax.sharding import PartitionSpec as P

HEAD = 64
KVH = 4
MOST = 2
PAGE = 128


EPS = 1e-06
THETA = 10000.0
BLOCK_ROWS = 512


def rms_scale(values, gain):
    values = values.astype(jnp.float32)
    mean_sq = jnp.mean(values * values, axis=-1, keepdims=True)
    return values * lax.rsqrt(mean_sq + EPS) * gain


def rope_tables(positions, width):
    half = width // 2
    inverse = THETA ** (-jnp.arange(half, dtype=jnp.float32) * 2.0 / width)
    angles = positions.astype(jnp.float32)[:, None] * inverse[None, :]
    return (jnp.cos(angles), jnp.sin(angles))


def rotate(values, cosine, sine):
    half = values.shape[-1] // 2
    first = values[..., :half]
    second = values[..., half:]
    cos_b = cosine[:, None, :]
    sin_b = sine[:, None, :]
    return jnp.concatenate(
        [first * cos_b - second * sin_b, second * cos_b + first * sin_b], axis=-1
    )


def segment_starts(seg_row):
    count = seg_row.shape[0]
    index = jnp.arange(count, dtype=jnp.int32)
    prior = jnp.concatenate([seg_row[:1] - 1, seg_row[:-1]])
    marks = jnp.where(seg_row != prior, index, 0)
    return lax.cummax(marks, axis=0)


def on_device(
    arrivals,
    deal,
    seg_ids,
    page_table,
    attn_gain,
    w_query,
    w_keyval,
    query_gain,
    key_gain,
    w_out,
    ffn_gain,
    w_gate,
    w_up,
    w_down,
):
    groups = lax.axis_size("dp")
    shards = lax.axis_size("tensor")
    tensor_rank = lax.axis_index("tensor")
    tok_grp = arrivals.shape[0]
    feat_part = arrivals.shape[1]
    units = deal.shape[1]
    unit_rows = tok_grp // units
    slot_count = groups * MOST
    width = unit_rows * feat_part
    dest_row = deal[0]
    target = dest_row // units
    unit_index = jnp.arange(units, dtype=jnp.int32)
    earlier = unit_index[:, None] > unit_index[None, :]
    same_target = target[:, None] == target[None, :]
    rank = jnp.sum(jnp.logical_and(earlier, same_target), axis=1)
    slot = target * MOST + rank
    slot_index = jnp.arange(slot_count, dtype=jnp.int32)
    send_hot = slot[None, :] == slot_index[:, None]
    send_src = jnp.sum(jnp.where(send_hot, unit_index[None, :], 0), axis=1)
    position = dest_row % units
    filled = jnp.any(send_hot, axis=1)
    slot_pos = jnp.where(filled, jnp.sum(jnp.where(send_hot, position[None, :], 0), axis=1), -1)
    pos_block = jnp.zeros((groups, 8, feat_part), jnp.bfloat16)
    pos_block = pos_block.at[:, 0, :MOST].set(slot_pos.reshape(groups, MOST).astype(jnp.bfloat16))
    arrival_units = arrivals.reshape(units, unit_rows, feat_part)
    packed = jnp.take(arrival_units, send_src, axis=0, mode="clip")
    payload = jnp.concatenate(
        [packed.reshape(groups, MOST * unit_rows, feat_part), pos_block], axis=1
    )
    received = lax.all_to_all(payload, "dp", split_axis=0, concat_axis=0, tiled=True)
    recv_pos = received[:, MOST * unit_rows, :MOST].reshape(slot_count).astype(jnp.int32)
    recv_units = received[:, : MOST * unit_rows].reshape(slot_count, unit_rows, feat_part)
    pos_hot = recv_pos[None, :] == unit_index[:, None]
    slot_of_pos = jnp.sum(jnp.where(pos_hot, slot_index[None, :], 0), axis=1)
    pos_of_slot = jnp.maximum(recv_pos, 0)
    grouped = jnp.take(recv_units, slot_of_pos, axis=0, mode="clip")
    grouped = grouped.reshape(tok_grp, feat_part)
    grouped, w_out = lax.optimization_barrier((grouped, w_out))
    w_out_full = lax.all_to_all(
        jnp.broadcast_to(w_out[None], (shards,) + w_out.shape), "tensor", 0, 0, tiled=True
    ).reshape(shards * w_out.shape[0], w_out.shape[1])
    full = lax.all_gather(grouped, "tensor", axis=1, tiled=True)
    normed = rms_scale(full, attn_gain).astype(jnp.bfloat16)
    seg_row = seg_ids[0]
    starts = segment_starts(seg_row)
    index = jnp.arange(tok_grp, dtype=jnp.int32)
    cosine, sine = rope_tables(index - starts, HEAD)
    q_heads = w_query.shape[1] // HEAD
    q_raw = jnp.dot(normed, w_query, preferred_element_type=jnp.float32).reshape(
        tok_grp, q_heads, HEAD
    )
    queries = rotate(rms_scale(q_raw, query_gain), cosine, sine).astype(jnp.bfloat16)
    kv_heads = max(1, KVH // shards)
    kv_first = tensor_rank * KVH // shards
    kv_weight = lax.dynamic_slice_in_dim(w_keyval, kv_first * 2 * HEAD, kv_heads * 2 * HEAD, 1)
    kv_raw = jnp.dot(normed, kv_weight, preferred_element_type=jnp.float32).reshape(
        tok_grp, kv_heads, 2, HEAD
    )
    keys = rotate(rms_scale(kv_raw[:, :, 0], key_gain), cosine, sine).astype(jnp.bfloat16)
    values = kv_raw[:, :, 1].astype(jnp.bfloat16)
    stacked = jnp.stack([keys, values], axis=2).reshape(tok_grp, kv_heads * 2 * HEAD)
    cache_cols = 2 * KVH * HEAD // shards
    offset = tensor_rank * cache_cols - kv_first * 2 * HEAD
    own_cache = lax.dynamic_slice_in_dim(stacked, offset, cache_cols, 1)
    pages = own_cache.reshape(tok_grp // PAGE, PAGE, cache_cols)
    kv_pages = jnp.zeros_like(pages).at[page_table[0]].set(pages)
    share = q_heads // kv_heads
    grouped_q = queries.reshape(tok_grp, kv_heads, share, HEAD)
    scale = 1.0 / math.sqrt(HEAD)
    block = min(BLOCK_ROWS, tok_grp)
    outputs = []
    for first in range(0, tok_grp, block):
        last = first + block
        scores = (
            jnp.einsum(
                "ikgd,jkd->kgij",
                grouped_q[first:last],
                keys[:last],
                preferred_element_type=jnp.float32,
            )
            * scale
        )
        query_rows = index[first:last]
        allowed = jnp.logical_and(
            query_rows[:, None] >= index[None, :last],
            starts[first:last][:, None] <= index[None, :last],
        )
        weights = jnp.where(allowed, jnp.exp(scores), 0.0)
        probs = (weights / jnp.sum(weights, axis=-1, keepdims=True)).astype(jnp.bfloat16)
        mixed = jnp.einsum(
            "kgij,jkd->ikgd", probs, values[:last], preferred_element_type=jnp.float32
        )
        outputs.append(mixed.astype(jnp.bfloat16).reshape(block, q_heads * HEAD))
    attended = jnp.concatenate(outputs, axis=0)
    attended_full = lax.all_gather(attended, "tensor", axis=1, tiled=True)
    attn_sum = jnp.dot(attended_full, w_out_full, preferred_element_type=jnp.float32)
    middle = (full.astype(jnp.float32) + attn_sum).astype(jnp.bfloat16)
    ffn_in = rms_scale(middle, ffn_gain).astype(jnp.bfloat16)
    gate = jnp.dot(ffn_in, w_gate, preferred_element_type=jnp.float32)
    upper = jnp.dot(ffn_in, w_up, preferred_element_type=jnp.float32)
    hidden = (jax.nn.silu(gate) * upper).astype(jnp.bfloat16)
    ffn_part = lax.psum_scatter(
        jnp.dot(hidden, w_down, preferred_element_type=jnp.float32).astype(jnp.bfloat16),
        "tensor",
        scatter_dimension=1,
        tiled=True,
    ).astype(jnp.float32)
    own_cols = lax.dynamic_slice_in_dim(middle, tensor_rank * feat_part, feat_part, 1)
    combined = (own_cols.astype(jnp.float32) + ffn_part).astype(jnp.bfloat16)
    back = jnp.take(combined.reshape(units, unit_rows, feat_part), pos_of_slot, axis=0, mode="clip")
    returned = lax.all_to_all(
        back.reshape(groups, MOST, unit_rows, feat_part), "dp", split_axis=0, concat_axis=0, tiled=True
    ).reshape(slot_count, unit_rows, feat_part)
    result = jnp.take(returned, slot, axis=0, mode="clip")
    return (result.reshape(tok_grp, feat_part), kv_pages)


def solution(mesh):
    return jax.shard_map(
        on_device,
        mesh=mesh,
        in_specs=(
            P("dp", "tensor"),
            P("dp", None),
            P("dp", None),
            P("dp", None),
            P(),
            P(None, "tensor"),
            P(),
            P(),
            P(),
            P("tensor", None),
            P(),
            P(None, "tensor"),
            P(None, "tensor"),
            P("tensor", None),
        ),
        out_specs=(P("dp", "tensor"), P("dp", None, "tensor")),
        check_vma=False,
    )
```

```python
import math

import jax
import jax.numpy as jnp
from jax import lax
from jax.sharding import PartitionSpec as P

HEAD = 64
KVH = 4
MOST = 2
PAGE = 128


EPS = 1e-06
THETA = 10000.0
BLOCK_ROWS = 512


def rms_scale(values, gain):
    values = values.astype(jnp.float32)
    mean_sq = jnp.mean(values * values, axis=-1, keepdims=True)
    return values * lax.rsqrt(mean_sq + EPS) * gain


def rope_tables(positions, width):
    half = width // 2
    inverse = THETA ** (-jnp.arange(half, dtype=jnp.float32) * 2.0 / width)
    angles = positions.astype(jnp.float32)[:, None] * inverse[None, :]
    return (jnp.cos(angles), jnp.sin(angles))


def rotate(values, cosine, sine):
    half = values.shape[-1] // 2
    first = values[..., :half]
    second = values[..., half:]
    cos_b = cosine[:, None, :]
    sin_b = sine[:, None, :]
    return jnp.concatenate(
        [first * cos_b - second * sin_b, second * cos_b + first * sin_b], axis=-1
    )


def segment_starts(seg_row):
    count = seg_row.shape[0]
    index = jnp.arange(count, dtype=jnp.int32)
    prior = jnp.concatenate([seg_row[:1] - 1, seg_row[:-1]])
    marks = jnp.where(seg_row != prior, index, 0)
    return lax.cummax(marks, axis=0)


def on_device(
    arrivals,
    deal,
    seg_ids,
    page_table,
    attn_gain,
    w_query,
    w_keyval,
    query_gain,
    key_gain,
    w_out,
    ffn_gain,
    w_gate,
    w_up,
    w_down,
):
    groups = lax.axis_size("dp")
    shards = lax.axis_size("tensor")
    tensor_rank = lax.axis_index("tensor")
    tok_grp = arrivals.shape[0]
    feat_part = arrivals.shape[1]
    units = deal.shape[1]
    unit_rows = tok_grp // units
    slot_count = groups * MOST
    width = unit_rows * feat_part
    dest_row = deal[0]
    target = dest_row // units
    unit_index = jnp.arange(units, dtype=jnp.int32)
    earlier = unit_index[:, None] > unit_index[None, :]
    same_target = target[:, None] == target[None, :]
    rank = jnp.sum(jnp.logical_and(earlier, same_target), axis=1)
    slot = target * MOST + rank
    slot_index = jnp.arange(slot_count, dtype=jnp.int32)
    send_hot = slot[None, :] == slot_index[:, None]
    send_src = jnp.sum(jnp.where(send_hot, unit_index[None, :], 0), axis=1)
    early_rows = w_out.shape[0] * 3 // 4
    w_out_early = lax.all_gather(w_out[:early_rows], "tensor", axis=0, tiled=False)
    position = dest_row % units
    filled = jnp.any(send_hot, axis=1)
    slot_pos = jnp.where(filled, jnp.sum(jnp.where(send_hot, position[None, :], 0), axis=1), -1)
    pos_block = jnp.zeros((groups, 8, feat_part), jnp.bfloat16)
    pos_block = pos_block.at[:, 0, :MOST].set(slot_pos.reshape(groups, MOST).astype(jnp.bfloat16))
    arrival_units = arrivals.reshape(units, unit_rows, feat_part)
    packed = jnp.take(arrival_units, send_src, axis=0, mode="clip")
    payload = jnp.concatenate(
        [packed.reshape(groups, MOST * unit_rows, feat_part), pos_block], axis=1
    )
    received = lax.all_to_all(payload, "dp", split_axis=0, concat_axis=0, tiled=True)
    recv_pos = received[:, MOST * unit_rows, :MOST].reshape(slot_count).astype(jnp.int32)
    recv_units = received[:, : MOST * unit_rows].reshape(slot_count, unit_rows, feat_part)
    pos_hot = recv_pos[None, :] == unit_index[:, None]
    slot_of_pos = jnp.sum(jnp.where(pos_hot, slot_index[None, :], 0), axis=1)
    pos_of_slot = jnp.maximum(recv_pos, 0)
    grouped = jnp.take(recv_units, slot_of_pos, axis=0, mode="clip")
    grouped = grouped.reshape(tok_grp, feat_part)
    grouped, w_out_early = lax.optimization_barrier((grouped, w_out_early))
    full = lax.all_gather(grouped, "tensor", axis=1, tiled=True)
    full, w_out_late = lax.optimization_barrier((full, w_out[early_rows:]))
    w_out_late = lax.all_gather(w_out_late, "tensor", axis=0, tiled=False)
    w_out_full = jnp.concatenate([w_out_early, w_out_late], axis=1).reshape(
        shards * w_out.shape[0], w_out.shape[1]
    )
    normed = rms_scale(full, attn_gain).astype(jnp.bfloat16)
    seg_row = seg_ids[0]
    starts = segment_starts(seg_row)
    index = jnp.arange(tok_grp, dtype=jnp.int32)
    cosine, sine = rope_tables(index - starts, HEAD)
    q_heads = w_query.shape[1] // HEAD
    q_raw = jnp.dot(normed, w_query, preferred_element_type=jnp.float32).reshape(
        tok_grp, q_heads, HEAD
    )
    queries = rotate(rms_scale(q_raw, query_gain), cosine, sine).astype(jnp.bfloat16)
    kv_heads = max(1, KVH // shards)
    kv_first = tensor_rank * KVH // shards
    kv_weight = lax.dynamic_slice_in_dim(w_keyval, kv_first * 2 * HEAD, kv_heads * 2 * HEAD, 1)
    kv_raw = jnp.dot(normed, kv_weight, preferred_element_type=jnp.float32).reshape(
        tok_grp, kv_heads, 2, HEAD
    )
    keys = rotate(rms_scale(kv_raw[:, :, 0], key_gain), cosine, sine).astype(jnp.bfloat16)
    values = kv_raw[:, :, 1].astype(jnp.bfloat16)
    stacked = jnp.stack([keys, values], axis=2).reshape(tok_grp, kv_heads * 2 * HEAD)
    cache_cols = 2 * KVH * HEAD // shards
    offset = tensor_rank * cache_cols - kv_first * 2 * HEAD
    own_cache = lax.dynamic_slice_in_dim(stacked, offset, cache_cols, 1)
    pages = own_cache.reshape(tok_grp // PAGE, PAGE, cache_cols)
    kv_pages = jnp.zeros_like(pages).at[page_table[0]].set(pages)
    share = q_heads // kv_heads
    grouped_q = queries.reshape(tok_grp, kv_heads, share, HEAD)
    scale = 1.0 / math.sqrt(HEAD)
    block = min(BLOCK_ROWS, tok_grp)
    outputs = []
    for first in range(0, tok_grp, block):
        last = first + block
        scores = (
            jnp.einsum(
                "ikgd,jkd->kgij",
                grouped_q[first:last],
                keys[:last],
                preferred_element_type=jnp.float32,
            )
            * scale
        )
        query_rows = index[first:last]
        allowed = jnp.logical_and(
            query_rows[:, None] >= index[None, :last],
            starts[first:last][:, None] <= index[None, :last],
        )
        weights = jnp.where(allowed, jnp.exp(scores), 0.0)
        probs = (weights / jnp.sum(weights, axis=-1, keepdims=True)).astype(jnp.bfloat16)
        mixed = jnp.einsum(
            "kgij,jkd->ikgd", probs, values[:last], preferred_element_type=jnp.float32
        )
        outputs.append(mixed.astype(jnp.bfloat16).reshape(block, q_heads * HEAD))
    attended = jnp.concatenate(outputs, axis=0)
    attended_full = lax.all_gather(attended, "tensor", axis=1, tiled=True)
    attn_sum = jnp.dot(attended_full, w_out_full, preferred_element_type=jnp.float32)
    middle = (full.astype(jnp.float32) + attn_sum).astype(jnp.bfloat16)
    ffn_in = rms_scale(middle, ffn_gain).astype(jnp.bfloat16)
    gate = jnp.dot(ffn_in, w_gate, preferred_element_type=jnp.float32)
    upper = jnp.dot(ffn_in, w_up, preferred_element_type=jnp.float32)
    hidden = (jax.nn.silu(gate) * upper).astype(jnp.bfloat16)
    ffn_part = lax.psum_scatter(
        jnp.dot(hidden, w_down, preferred_element_type=jnp.float32).astype(jnp.bfloat16),
        "tensor",
        scatter_dimension=1,
        tiled=True,
    ).astype(jnp.float32)
    own_cols = lax.dynamic_slice_in_dim(middle, tensor_rank * feat_part, feat_part, 1)
    combined = (own_cols.astype(jnp.float32) + ffn_part).astype(jnp.bfloat16)
    back = jnp.take(combined.reshape(units, unit_rows, feat_part), pos_of_slot, axis=0, mode="clip")
    returned = lax.all_to_all(
        back.reshape(groups, MOST, unit_rows, feat_part), "dp", split_axis=0, concat_axis=0, tiled=True
    ).reshape(slot_count, unit_rows, feat_part)
    result = jnp.take(returned, slot, axis=0, mode="clip")
    return (result.reshape(tok_grp, feat_part), kv_pages)


def solution(mesh):
    return jax.shard_map(
        on_device,
        mesh=mesh,
        in_specs=(
            P("dp", "tensor"),
            P("dp", None),
            P("dp", None),
            P("dp", None),
            P(),
            P(None, "tensor"),
            P(),
            P(),
            P(),
            P("tensor", None),
            P(),
            P(None, "tensor"),
            P(None, "tensor"),
            P("tensor", None),
        ),
        out_specs=(P("dp", "tensor"), P("dp", None, "tensor")),
        check_vma=False,
    )
```

```python
import math

import jax
import jax.numpy as jnp
from jax import lax
from jax.sharding import PartitionSpec as P

HEAD = 64
KVH = 4
MOST = 2
PAGE = 128


EPS = 1e-06
THETA = 10000.0
BLOCK_ROWS = 512


def rms_scale(values, gain):
    values = values.astype(jnp.float32)
    mean_sq = jnp.mean(values * values, axis=-1, keepdims=True)
    return values * lax.rsqrt(mean_sq + EPS) * gain


def rope_tables(positions, width):
    half = width // 2
    inverse = THETA ** (-jnp.arange(half, dtype=jnp.float32) * 2.0 / width)
    angles = positions.astype(jnp.float32)[:, None] * inverse[None, :]
    return (jnp.cos(angles), jnp.sin(angles))


def rotate(values, cosine, sine):
    half = values.shape[-1] // 2
    first = values[..., :half]
    second = values[..., half:]
    cos_b = cosine[:, None, :]
    sin_b = sine[:, None, :]
    return jnp.concatenate(
        [first * cos_b - second * sin_b, second * cos_b + first * sin_b], axis=-1
    )


def segment_starts(seg_row):
    count = seg_row.shape[0]
    index = jnp.arange(count, dtype=jnp.int32)
    prior = jnp.concatenate([seg_row[:1] - 1, seg_row[:-1]])
    marks = jnp.where(seg_row != prior, index, 0)
    return lax.cummax(marks, axis=0)


def on_device(
    arrivals,
    deal,
    seg_ids,
    page_table,
    attn_gain,
    w_query,
    w_keyval,
    query_gain,
    key_gain,
    w_out,
    ffn_gain,
    w_gate,
    w_up,
    w_down,
):
    groups = lax.axis_size("dp")
    shards = lax.axis_size("tensor")
    tensor_rank = lax.axis_index("tensor")
    tok_grp = arrivals.shape[0]
    feat_part = arrivals.shape[1]
    units = deal.shape[1]
    unit_rows = tok_grp // units
    slot_count = groups * MOST
    width = unit_rows * feat_part
    dest_row = deal[0]
    target = dest_row // units
    unit_index = jnp.arange(units, dtype=jnp.int32)
    earlier = unit_index[:, None] > unit_index[None, :]
    same_target = target[:, None] == target[None, :]
    rank = jnp.sum(jnp.logical_and(earlier, same_target), axis=1)
    slot = target * MOST + rank
    slot_index = jnp.arange(slot_count, dtype=jnp.int32)
    send_hot = slot[None, :] == slot_index[:, None]
    send_src = jnp.sum(jnp.where(send_hot, unit_index[None, :], 0), axis=1)
    w_out_full = lax.all_gather(w_out, "tensor", axis=0, tiled=True)
    position = dest_row % units
    filled = jnp.any(send_hot, axis=1)
    slot_pos = jnp.where(filled, jnp.sum(jnp.where(send_hot, position[None, :], 0), axis=1), -1)
    pos_block = jnp.zeros((groups, 8, feat_part), jnp.bfloat16)
    pos_block = pos_block.at[:, 0, :MOST].set(slot_pos.reshape(groups, MOST).astype(jnp.bfloat16))
    arrival_units = arrivals.reshape(units, unit_rows, feat_part)
    packed = jnp.take(arrival_units, send_src, axis=0, mode="clip")
    payload = jnp.concatenate(
        [packed.reshape(groups, MOST * unit_rows, feat_part), pos_block], axis=1
    )
    received = lax.all_to_all(payload, "dp", split_axis=0, concat_axis=0, tiled=True)
    recv_pos = received[:, MOST * unit_rows, :MOST].reshape(slot_count).astype(jnp.int32)
    recv_units = received[:, : MOST * unit_rows].reshape(slot_count, unit_rows, feat_part)
    pos_hot = recv_pos[None, :] == unit_index[:, None]
    slot_of_pos = jnp.sum(jnp.where(pos_hot, slot_index[None, :], 0), axis=1)
    pos_of_slot = jnp.maximum(recv_pos, 0)
    grouped = jnp.take(recv_units, slot_of_pos, axis=0, mode="clip")
    grouped = grouped.reshape(tok_grp, feat_part)
    grouped, w_out_full = lax.optimization_barrier((grouped, w_out_full))
    full = lax.all_gather(grouped, "tensor", axis=1, tiled=True)
    normed = rms_scale(full, attn_gain).astype(jnp.bfloat16)
    seg_row = seg_ids[0]
    starts = segment_starts(seg_row)
    index = jnp.arange(tok_grp, dtype=jnp.int32)
    cosine, sine = rope_tables(index - starts, HEAD)
    q_heads = w_query.shape[1] // HEAD
    kv_heads = max(1, KVH // shards)
    kv_first = tensor_rank * KVH // shards
    kv_weight = lax.dynamic_slice_in_dim(w_keyval, kv_first * 2 * HEAD, kv_heads * 2 * HEAD, 1)
    qkv_weight = jnp.concatenate([w_query, kv_weight], axis=1)
    qkv_raw = jnp.dot(normed, qkv_weight, preferred_element_type=jnp.float32)
    q_cols = w_query.shape[1]
    q_raw = qkv_raw[:, :q_cols].reshape(tok_grp, q_heads, HEAD)
    queries = rotate(rms_scale(q_raw, query_gain), cosine, sine).astype(jnp.bfloat16)
    kv_raw = qkv_raw[:, q_cols:].reshape(tok_grp, kv_heads, 2, HEAD)
    keys = rotate(rms_scale(kv_raw[:, :, 0], key_gain), cosine, sine).astype(jnp.bfloat16)
    values = kv_raw[:, :, 1].astype(jnp.bfloat16)
    stacked = jnp.stack([keys, values], axis=2).reshape(tok_grp, kv_heads * 2 * HEAD)
    cache_cols = 2 * KVH * HEAD // shards
    offset = tensor_rank * cache_cols - kv_first * 2 * HEAD
    own_cache = lax.dynamic_slice_in_dim(stacked, offset, cache_cols, 1)
    pages = own_cache.reshape(tok_grp // PAGE, PAGE, cache_cols)
    kv_pages = jnp.zeros_like(pages).at[page_table[0]].set(pages)
    share = q_heads // kv_heads
    grouped_q = queries.reshape(tok_grp, kv_heads, share, HEAD)
    scale = 1.0 / math.sqrt(HEAD)
    block = min(BLOCK_ROWS, tok_grp)
    outputs = []
    for first in range(0, tok_grp, block):
        last = first + block
        scores = (
            jnp.einsum(
                "ikgd,jkd->kgij",
                grouped_q[first:last],
                keys[:last],
                preferred_element_type=jnp.float32,
            )
            * scale
        )
        query_rows = index[first:last]
        allowed = jnp.logical_and(
            query_rows[:, None] >= index[None, :last],
            starts[first:last][:, None] <= index[None, :last],
        )
        weights = jnp.where(allowed, jnp.exp(scores), 0.0)
        probs = (weights / jnp.sum(weights, axis=-1, keepdims=True)).astype(jnp.bfloat16)
        mixed = jnp.einsum(
            "kgij,jkd->ikgd", probs, values[:last], preferred_element_type=jnp.float32
        )
        outputs.append(mixed.astype(jnp.bfloat16).reshape(block, q_heads * HEAD))
    attended = jnp.concatenate(outputs, axis=0)
    attended_full = lax.all_gather(attended, "tensor", axis=1, tiled=True)
    attn_sum = jnp.dot(attended_full, w_out_full, preferred_element_type=jnp.float32)
    middle = (full.astype(jnp.float32) + attn_sum).astype(jnp.bfloat16)
    ffn_in = rms_scale(middle, ffn_gain).astype(jnp.bfloat16)
    ff_part = w_gate.shape[1]
    gate_up = jnp.dot(
        ffn_in, jnp.concatenate([w_gate, w_up], axis=1), preferred_element_type=jnp.float32
    )
    gate = gate_up[:, :ff_part]
    upper = gate_up[:, ff_part:]
    hidden = (jax.nn.silu(gate) * upper).astype(jnp.bfloat16)
    ffn_part = lax.psum_scatter(
        jnp.dot(hidden, w_down, preferred_element_type=jnp.float32).astype(jnp.bfloat16),
        "tensor",
        scatter_dimension=1,
        tiled=True,
    ).astype(jnp.float32)
    own_cols = lax.dynamic_slice_in_dim(middle, tensor_rank * feat_part, feat_part, 1)
    combined = (own_cols.astype(jnp.float32) + ffn_part).astype(jnp.bfloat16)
    back = jnp.take(combined.reshape(units, unit_rows, feat_part), pos_of_slot, axis=0, mode="clip")
    returned = lax.all_to_all(
        back.reshape(groups, MOST, unit_rows, feat_part), "dp", split_axis=0, concat_axis=0, tiled=True
    ).reshape(slot_count, unit_rows, feat_part)
    result = jnp.take(returned, slot, axis=0, mode="clip")
    return (result.reshape(tok_grp, feat_part), kv_pages)


def solution(mesh):
    return jax.shard_map(
        on_device,
        mesh=mesh,
        in_specs=(
            P("dp", "tensor"),
            P("dp", None),
            P("dp", None),
            P("dp", None),
            P(),
            P(None, "tensor"),
            P(),
            P(),
            P(),
            P("tensor", None),
            P(),
            P(None, "tensor"),
            P(None, "tensor"),
            P("tensor", None),
        ),
        out_specs=(P("dp", "tensor"), P("dp", None, "tensor")),
        check_vma=False,
    )
```

```python
import math

import jax
import jax.numpy as jnp
from jax import lax
from jax.sharding import PartitionSpec as P

HEAD = 64
KVH = 4
MOST = 2
PAGE = 128


EPS = 1e-06
THETA = 10000.0
BLOCK_ROWS = 512


def rms_scale(values, gain):
    values = values.astype(jnp.float32)
    mean_sq = jnp.mean(values * values, axis=-1, keepdims=True)
    return values * lax.rsqrt(mean_sq + EPS) * gain


def rope_tables(positions, width):
    half = width // 2
    inverse = THETA ** (-jnp.arange(half, dtype=jnp.float32) * 2.0 / width)
    angles = positions.astype(jnp.float32)[:, None] * inverse[None, :]
    return (jnp.cos(angles), jnp.sin(angles))


def rotate(values, cosine, sine):
    half = values.shape[-1] // 2
    first = values[..., :half]
    second = values[..., half:]
    cos_b = cosine[:, None, :]
    sin_b = sine[:, None, :]
    return jnp.concatenate(
        [first * cos_b - second * sin_b, second * cos_b + first * sin_b], axis=-1
    )


def segment_starts(seg_row):
    count = seg_row.shape[0]
    index = jnp.arange(count, dtype=jnp.int32)
    prior = jnp.concatenate([seg_row[:1] - 1, seg_row[:-1]])
    marks = jnp.where(seg_row != prior, index, 0)
    return lax.cummax(marks, axis=0)


def on_device(
    arrivals,
    deal,
    seg_ids,
    page_table,
    attn_gain,
    w_query,
    w_keyval,
    query_gain,
    key_gain,
    w_out,
    ffn_gain,
    w_gate,
    w_up,
    w_down,
):
    groups = lax.axis_size("dp")
    shards = lax.axis_size("tensor")
    tensor_rank = lax.axis_index("tensor")
    tok_grp = arrivals.shape[0]
    feat_part = arrivals.shape[1]
    units = deal.shape[1]
    unit_rows = tok_grp // units
    slot_count = groups * MOST
    width = unit_rows * feat_part
    dest_row = deal[0]
    target = dest_row // units
    unit_index = jnp.arange(units, dtype=jnp.int32)
    earlier = unit_index[:, None] > unit_index[None, :]
    same_target = target[:, None] == target[None, :]
    rank = jnp.sum(jnp.logical_and(earlier, same_target), axis=1)
    slot = target * MOST + rank
    slot_index = jnp.arange(slot_count, dtype=jnp.int32)
    send_hot = slot[None, :] == slot_index[:, None]
    send_src = jnp.sum(jnp.where(send_hot, unit_index[None, :], 0), axis=1)
    w_out_full = lax.all_gather(w_out, "tensor", axis=0, tiled=True)
    position = dest_row % units
    filled = jnp.any(send_hot, axis=1)
    slot_pos = jnp.where(filled, jnp.sum(jnp.where(send_hot, position[None, :], 0), axis=1), -1)
    pos_block = jnp.zeros((groups, 8, feat_part), jnp.bfloat16)
    pos_block = pos_block.at[:, 0, :MOST].set(slot_pos.reshape(groups, MOST).astype(jnp.bfloat16))
    arrival_units = arrivals.reshape(units, unit_rows, feat_part)
    packed = jnp.take(arrival_units, send_src, axis=0, mode="clip")
    payload = jnp.concatenate(
        [packed.reshape(groups, MOST * unit_rows, feat_part), pos_block], axis=1
    )
    received = lax.all_to_all(payload, "dp", split_axis=0, concat_axis=0, tiled=True)
    recv_pos = received[:, MOST * unit_rows, :MOST].reshape(slot_count).astype(jnp.int32)
    recv_units = received[:, : MOST * unit_rows].reshape(slot_count, unit_rows, feat_part)
    pos_hot = recv_pos[None, :] == unit_index[:, None]
    slot_of_pos = jnp.sum(jnp.where(pos_hot, slot_index[None, :], 0), axis=1)
    pos_of_slot = jnp.maximum(recv_pos, 0)
    grouped = jnp.take(recv_units, slot_of_pos, axis=0, mode="clip")
    grouped = grouped.reshape(tok_grp, feat_part)
    grouped, w_out_full = lax.optimization_barrier((grouped, w_out_full))
    full = lax.all_gather(grouped, "tensor", axis=1, tiled=True)
    normed = rms_scale(full, attn_gain).astype(jnp.bfloat16)
    seg_row = seg_ids[0]
    starts = segment_starts(seg_row)
    index = jnp.arange(tok_grp, dtype=jnp.int32)
    cosine, sine = rope_tables(index - starts, HEAD)
    q_heads = w_query.shape[1] // HEAD
    kv_heads = max(1, KVH // shards)
    kv_first = tensor_rank * KVH // shards
    kv_weight = lax.dynamic_slice_in_dim(w_keyval, kv_first * 2 * HEAD, kv_heads * 2 * HEAD, 1)
    qkv_weight = jnp.concatenate([w_query, kv_weight], axis=1)
    qkv_raw = jnp.dot(normed, qkv_weight, preferred_element_type=jnp.float32)
    q_cols = w_query.shape[1]
    q_raw = qkv_raw[:, :q_cols].reshape(tok_grp, q_heads, HEAD)
    queries = rotate(rms_scale(q_raw, query_gain), cosine, sine).astype(jnp.bfloat16)
    kv_raw = qkv_raw[:, q_cols:].reshape(tok_grp, kv_heads, 2, HEAD)
    keys = rotate(rms_scale(kv_raw[:, :, 0], key_gain), cosine, sine).astype(jnp.bfloat16)
    values = kv_raw[:, :, 1].astype(jnp.bfloat16)
    stacked = jnp.stack([keys, values], axis=2).reshape(tok_grp, kv_heads * 2 * HEAD)
    cache_cols = 2 * KVH * HEAD // shards
    offset = tensor_rank * cache_cols - kv_first * 2 * HEAD
    own_cache = lax.dynamic_slice_in_dim(stacked, offset, cache_cols, 1)
    pages = own_cache.reshape(tok_grp // PAGE, PAGE, cache_cols)
    kv_pages = jnp.zeros_like(pages).at[page_table[0]].set(pages)
    share = q_heads // kv_heads
    grouped_q = queries.reshape(tok_grp, kv_heads, share, HEAD)
    scale = 1.0 / math.sqrt(HEAD)
    block = min(BLOCK_ROWS, tok_grp)
    outputs = []
    for first in range(0, tok_grp, block):
        last = first + block
        scores = (
            jnp.einsum(
                "ikgd,jkd->kgij",
                grouped_q[first:last],
                keys[:last],
                preferred_element_type=jnp.float32,
            )
            * scale
        )
        query_rows = index[first:last]
        allowed = jnp.logical_and(
            query_rows[:, None] >= index[None, :last],
            starts[first:last][:, None] <= index[None, :last],
        )
        weights = jnp.where(allowed, jnp.exp(scores), 0.0)
        probs = (weights / jnp.sum(weights, axis=-1, keepdims=True)).astype(jnp.bfloat16)
        mixed = jnp.einsum(
            "kgij,jkd->ikgd", probs, values[:last], preferred_element_type=jnp.float32
        )
        outputs.append(mixed.astype(jnp.bfloat16).reshape(block, q_heads * HEAD))
    attended = jnp.concatenate(outputs, axis=0)
    attended_full = lax.all_gather(attended, "tensor", axis=1, tiled=True)
    attn_sum = jnp.dot(attended_full, w_out_full, preferred_element_type=jnp.float32)
    attn_sum = lax.optimization_barrier(attn_sum.astype(jnp.bfloat16)).astype(jnp.float32)
    middle = (full.astype(jnp.float32) + attn_sum).astype(jnp.bfloat16)
    ffn_in = rms_scale(middle, ffn_gain).astype(jnp.bfloat16)
    ff_part = w_gate.shape[1]
    gate_up = jnp.dot(
        ffn_in, jnp.concatenate([w_gate, w_up], axis=1), preferred_element_type=jnp.float32
    )
    gate = gate_up[:, :ff_part]
    upper = gate_up[:, ff_part:]
    hidden = lax.optimization_barrier((jax.nn.silu(gate) * upper).astype(jnp.bfloat16))
    ffn_part = lax.psum_scatter(
        jnp.dot(hidden, w_down, preferred_element_type=jnp.float32).astype(jnp.bfloat16),
        "tensor",
        scatter_dimension=1,
        tiled=True,
    ).astype(jnp.float32)
    own_cols = lax.dynamic_slice_in_dim(middle, tensor_rank * feat_part, feat_part, 1)
    combined = (own_cols.astype(jnp.float32) + ffn_part).astype(jnp.bfloat16)
    back = jnp.take(combined.reshape(units, unit_rows, feat_part), pos_of_slot, axis=0, mode="clip")
    returned = lax.all_to_all(
        back.reshape(groups, MOST, unit_rows, feat_part), "dp", split_axis=0, concat_axis=0, tiled=True
    ).reshape(slot_count, unit_rows, feat_part)
    result = jnp.take(returned, slot, axis=0, mode="clip")
    return (result.reshape(tok_grp, feat_part), kv_pages)


def solution(mesh):
    return jax.shard_map(
        on_device,
        mesh=mesh,
        in_specs=(
            P("dp", "tensor"),
            P("dp", None),
            P("dp", None),
            P("dp", None),
            P(),
            P(None, "tensor"),
            P(),
            P(),
            P(),
            P("tensor", None),
            P(),
            P(None, "tensor"),
            P(None, "tensor"),
            P("tensor", None),
        ),
        out_specs=(P("dp", "tensor"), P("dp", None, "tensor")),
        check_vma=False,
    )
```

```python
import math

import jax
import jax.numpy as jnp
from jax import lax
from jax.sharding import PartitionSpec as P

HEAD = 64
KVH = 4
MOST = 2
PAGE = 128


EPS = 1e-06
THETA = 10000.0
BLOCK_ROWS = 256
LONGEST = 512


def rms_scale(values, gain):
    values = values.astype(jnp.float32)
    mean_sq = jnp.mean(values * values, axis=-1, keepdims=True)
    return values * lax.rsqrt(mean_sq + EPS) * gain


def rope_tables(positions, width):
    half = width // 2
    inverse = THETA ** (-jnp.arange(half, dtype=jnp.float32) * 2.0 / width)
    angles = positions.astype(jnp.float32)[:, None] * inverse[None, :]
    return (jnp.cos(angles), jnp.sin(angles))


def rotate(values, cosine, sine):
    half = values.shape[-1] // 2
    first = values[..., :half]
    second = values[..., half:]
    cos_b = cosine[:, None, :]
    sin_b = sine[:, None, :]
    return jnp.concatenate(
        [first * cos_b - second * sin_b, second * cos_b + first * sin_b], axis=-1
    )


def segment_starts(seg_row):
    count = seg_row.shape[0]
    index = jnp.arange(count, dtype=jnp.int32)
    prior = jnp.concatenate([seg_row[:1] - 1, seg_row[:-1]])
    marks = jnp.where(seg_row != prior, index, 0)
    return lax.cummax(marks, axis=0)


def on_device(
    arrivals,
    deal,
    seg_ids,
    page_table,
    attn_gain,
    w_query,
    w_keyval,
    query_gain,
    key_gain,
    w_out,
    ffn_gain,
    w_gate,
    w_up,
    w_down,
):
    groups = lax.axis_size("dp")
    shards = lax.axis_size("tensor")
    tensor_rank = lax.axis_index("tensor")
    tok_grp = arrivals.shape[0]
    feat_part = arrivals.shape[1]
    units = deal.shape[1]
    unit_rows = tok_grp // units
    slot_count = groups * MOST
    width = unit_rows * feat_part
    dest_row = deal[0]
    target = dest_row // units
    unit_index = jnp.arange(units, dtype=jnp.int32)
    earlier = unit_index[:, None] > unit_index[None, :]
    same_target = target[:, None] == target[None, :]
    rank = jnp.sum(jnp.logical_and(earlier, same_target), axis=1)
    slot = target * MOST + rank
    slot_index = jnp.arange(slot_count, dtype=jnp.int32)
    send_hot = slot[None, :] == slot_index[:, None]
    send_src = jnp.sum(jnp.where(send_hot, unit_index[None, :], 0), axis=1)
    w_out_full = lax.all_gather(w_out, "tensor", axis=0, tiled=True)
    position = dest_row % units
    filled = jnp.any(send_hot, axis=1)
    slot_pos = jnp.where(filled, jnp.sum(jnp.where(send_hot, position[None, :], 0), axis=1), -1)
    pos_block = jnp.zeros((groups, 8, feat_part), jnp.bfloat16)
    pos_block = pos_block.at[:, 0, :MOST].set(slot_pos.reshape(groups, MOST).astype(jnp.bfloat16))
    arrival_units = arrivals.reshape(units, unit_rows, feat_part)
    packed = jnp.take(arrival_units, send_src, axis=0, mode="clip")
    payload = jnp.concatenate(
        [packed.reshape(groups, MOST * unit_rows, feat_part), pos_block], axis=1
    )
    received = lax.all_to_all(payload, "dp", split_axis=0, concat_axis=0, tiled=True)
    recv_pos = received[:, MOST * unit_rows, :MOST].reshape(slot_count).astype(jnp.int32)
    recv_units = received[:, : MOST * unit_rows].reshape(slot_count, unit_rows, feat_part)
    pos_hot = recv_pos[None, :] == unit_index[:, None]
    slot_of_pos = jnp.sum(jnp.where(pos_hot, slot_index[None, :], 0), axis=1)
    pos_of_slot = jnp.maximum(recv_pos, 0)
    grouped = jnp.take(recv_units, slot_of_pos, axis=0, mode="clip")
    grouped = grouped.reshape(tok_grp, feat_part)
    grouped, w_out_full = lax.optimization_barrier((grouped, w_out_full))
    full = lax.all_gather(grouped, "tensor", axis=1, tiled=True)
    normed = rms_scale(full, attn_gain).astype(jnp.bfloat16)
    seg_row = seg_ids[0]
    starts = segment_starts(seg_row)
    index = jnp.arange(tok_grp, dtype=jnp.int32)
    cosine, sine = rope_tables(index - starts, HEAD)
    q_heads = w_query.shape[1] // HEAD
    kv_heads = max(1, KVH // shards)
    kv_first = tensor_rank * KVH // shards
    kv_weight = lax.dynamic_slice_in_dim(w_keyval, kv_first * 2 * HEAD, kv_heads * 2 * HEAD, 1)
    qkv_weight = jnp.concatenate([w_query, kv_weight], axis=1)
    qkv_raw = jnp.dot(normed, qkv_weight, preferred_element_type=jnp.float32)
    q_cols = w_query.shape[1]
    q_raw = qkv_raw[:, :q_cols].reshape(tok_grp, q_heads, HEAD)
    queries = rotate(rms_scale(q_raw, query_gain), cosine, sine).astype(jnp.bfloat16)
    kv_raw = qkv_raw[:, q_cols:].reshape(tok_grp, kv_heads, 2, HEAD)
    keys = rotate(rms_scale(kv_raw[:, :, 0], key_gain), cosine, sine).astype(jnp.bfloat16)
    values = kv_raw[:, :, 1].astype(jnp.bfloat16)
    stacked = jnp.stack([keys, values], axis=2).reshape(tok_grp, kv_heads * 2 * HEAD)
    cache_cols = 2 * KVH * HEAD // shards
    offset = tensor_rank * cache_cols - kv_first * 2 * HEAD
    own_cache = lax.dynamic_slice_in_dim(stacked, offset, cache_cols, 1)
    pages = own_cache.reshape(tok_grp // PAGE, PAGE, cache_cols)
    kv_pages = jnp.zeros_like(pages).at[page_table[0]].set(pages)
    share = q_heads // kv_heads
    grouped_q = queries.reshape(tok_grp, kv_heads, share, HEAD)
    scale = 1.0 / math.sqrt(HEAD)
    block = min(BLOCK_ROWS, tok_grp)
    outputs = []
    for first in range(0, tok_grp, block):
        last = first + block
        low = max(0, (first - LONGEST) // block * block)
        scores = (
            jnp.einsum(
                "ikgd,jkd->kgij",
                grouped_q[first:last],
                keys[low:last],
                preferred_element_type=jnp.float32,
            )
            * scale
        )
        query_rows = index[first:last]
        allowed = jnp.logical_and(
            query_rows[:, None] >= index[None, low:last],
            starts[first:last][:, None] <= index[None, low:last],
        )
        weights = jnp.where(allowed, jnp.exp(scores), 0.0)
        probs = (weights / jnp.sum(weights, axis=-1, keepdims=True)).astype(jnp.bfloat16)
        mixed = jnp.einsum(
            "kgij,jkd->ikgd", probs, values[low:last], preferred_element_type=jnp.float32
        )
        outputs.append(mixed.astype(jnp.bfloat16).reshape(block, q_heads * HEAD))
    attended = jnp.concatenate(outputs, axis=0)
    attended_full = lax.all_gather(attended, "tensor", axis=1, tiled=True)
    attn_sum = jnp.dot(attended_full, w_out_full, preferred_element_type=jnp.float32)
    middle = (full.astype(jnp.float32) + attn_sum).astype(jnp.bfloat16)
    ffn_in = rms_scale(middle, ffn_gain).astype(jnp.bfloat16)
    ff_part = w_gate.shape[1]
    gate_up = jnp.dot(
        ffn_in, jnp.concatenate([w_gate, w_up], axis=1), preferred_element_type=jnp.float32
    )
    gate = gate_up[:, :ff_part]
    upper = gate_up[:, ff_part:]
    hidden = (jax.nn.silu(gate) * upper).astype(jnp.bfloat16)
    ffn_part = lax.psum_scatter(
        jnp.dot(hidden, w_down, preferred_element_type=jnp.float32).astype(jnp.bfloat16),
        "tensor",
        scatter_dimension=1,
        tiled=True,
    ).astype(jnp.float32)
    own_cols = lax.dynamic_slice_in_dim(middle, tensor_rank * feat_part, feat_part, 1)
    combined = (own_cols.astype(jnp.float32) + ffn_part).astype(jnp.bfloat16)
    back = jnp.take(combined.reshape(units, unit_rows, feat_part), pos_of_slot, axis=0, mode="clip")
    returned = lax.all_to_all(
        back.reshape(groups, MOST, unit_rows, feat_part), "dp", split_axis=0, concat_axis=0, tiled=True
    ).reshape(slot_count, unit_rows, feat_part)
    result = jnp.take(returned, slot, axis=0, mode="clip")
    return (result.reshape(tok_grp, feat_part), kv_pages)


def solution(mesh):
    return jax.shard_map(
        on_device,
        mesh=mesh,
        in_specs=(
            P("dp", "tensor"),
            P("dp", None),
            P("dp", None),
            P("dp", None),
            P(),
            P(None, "tensor"),
            P(),
            P(),
            P(),
            P("tensor", None),
            P(),
            P(None, "tensor"),
            P(None, "tensor"),
            P("tensor", None),
        ),
        out_specs=(P("dp", "tensor"), P("dp", None, "tensor")),
        check_vma=False,
    )
```

```python
import math

import jax
import jax.numpy as jnp
from jax import lax
from jax.sharding import PartitionSpec as P

HEAD = 64
KVH = 4
MOST = 2
PAGE = 128


EPS = 1e-06
THETA = 10000.0
BLOCK_ROWS = 128
LONGEST = 512


def rms_scale(values, gain):
    values = values.astype(jnp.float32)
    mean_sq = jnp.mean(values * values, axis=-1, keepdims=True)
    return values * lax.rsqrt(mean_sq + EPS) * gain


def rope_tables(positions, width):
    half = width // 2
    inverse = THETA ** (-jnp.arange(half, dtype=jnp.float32) * 2.0 / width)
    angles = positions.astype(jnp.float32)[:, None] * inverse[None, :]
    return (jnp.cos(angles), jnp.sin(angles))


def rotate(values, cosine, sine):
    half = values.shape[-1] // 2
    first = values[..., :half]
    second = values[..., half:]
    cos_b = cosine[:, None, :]
    sin_b = sine[:, None, :]
    return jnp.concatenate(
        [first * cos_b - second * sin_b, second * cos_b + first * sin_b], axis=-1
    )


def segment_starts(seg_row):
    count = seg_row.shape[0]
    index = jnp.arange(count, dtype=jnp.int32)
    prior = jnp.concatenate([seg_row[:1] - 1, seg_row[:-1]])
    marks = jnp.where(seg_row != prior, index, 0)
    return lax.cummax(marks, axis=0)


def on_device(
    arrivals,
    deal,
    seg_ids,
    page_table,
    attn_gain,
    w_query,
    w_keyval,
    query_gain,
    key_gain,
    w_out,
    ffn_gain,
    w_gate,
    w_up,
    w_down,
):
    groups = lax.axis_size("dp")
    shards = lax.axis_size("tensor")
    tensor_rank = lax.axis_index("tensor")
    tok_grp = arrivals.shape[0]
    feat_part = arrivals.shape[1]
    units = deal.shape[1]
    unit_rows = tok_grp // units
    slot_count = groups * MOST
    width = unit_rows * feat_part
    dest_row = deal[0]
    target = dest_row // units
    unit_index = jnp.arange(units, dtype=jnp.int32)
    earlier = unit_index[:, None] > unit_index[None, :]
    same_target = target[:, None] == target[None, :]
    rank = jnp.sum(jnp.logical_and(earlier, same_target), axis=1)
    slot = target * MOST + rank
    slot_index = jnp.arange(slot_count, dtype=jnp.int32)
    send_hot = slot[None, :] == slot_index[:, None]
    send_src = jnp.sum(jnp.where(send_hot, unit_index[None, :], 0), axis=1)
    w_out_full = lax.all_gather(w_out, "tensor", axis=0, tiled=True)
    position = dest_row % units
    filled = jnp.any(send_hot, axis=1)
    slot_pos = jnp.where(filled, jnp.sum(jnp.where(send_hot, position[None, :], 0), axis=1), -1)
    pos_block = jnp.zeros((groups, 8, feat_part), jnp.bfloat16)
    pos_block = pos_block.at[:, 0, :MOST].set(slot_pos.reshape(groups, MOST).astype(jnp.bfloat16))
    arrival_units = arrivals.reshape(units, unit_rows, feat_part)
    packed = jnp.take(arrival_units, send_src, axis=0, mode="clip")
    payload = jnp.concatenate(
        [packed.reshape(groups, MOST * unit_rows, feat_part), pos_block], axis=1
    )
    received = lax.all_to_all(payload, "dp", split_axis=0, concat_axis=0, tiled=True)
    recv_pos = received[:, MOST * unit_rows, :MOST].reshape(slot_count).astype(jnp.int32)
    recv_units = received[:, : MOST * unit_rows].reshape(slot_count, unit_rows, feat_part)
    pos_hot = recv_pos[None, :] == unit_index[:, None]
    slot_of_pos = jnp.sum(jnp.where(pos_hot, slot_index[None, :], 0), axis=1)
    pos_of_slot = jnp.maximum(recv_pos, 0)
    grouped = jnp.take(recv_units, slot_of_pos, axis=0, mode="clip")
    grouped = grouped.reshape(tok_grp, feat_part)
    grouped, w_out_full = lax.optimization_barrier((grouped, w_out_full))
    full = lax.all_gather(grouped, "tensor", axis=1, tiled=True)
    normed = rms_scale(full, attn_gain).astype(jnp.bfloat16)
    seg_row = seg_ids[0]
    starts = segment_starts(seg_row)
    index = jnp.arange(tok_grp, dtype=jnp.int32)
    cosine, sine = rope_tables(index - starts, HEAD)
    q_heads = w_query.shape[1] // HEAD
    kv_heads = max(1, KVH // shards)
    kv_first = tensor_rank * KVH // shards
    kv_weight = lax.dynamic_slice_in_dim(w_keyval, kv_first * 2 * HEAD, kv_heads * 2 * HEAD, 1)
    qkv_weight = jnp.concatenate([w_query, kv_weight], axis=1)
    qkv_raw = jnp.dot(normed, qkv_weight, preferred_element_type=jnp.float32)
    q_cols = w_query.shape[1]
    q_raw = qkv_raw[:, :q_cols].reshape(tok_grp, q_heads, HEAD)
    queries = rotate(rms_scale(q_raw, query_gain), cosine, sine).astype(jnp.bfloat16)
    kv_raw = qkv_raw[:, q_cols:].reshape(tok_grp, kv_heads, 2, HEAD)
    keys = rotate(rms_scale(kv_raw[:, :, 0], key_gain), cosine, sine).astype(jnp.bfloat16)
    values = kv_raw[:, :, 1].astype(jnp.bfloat16)
    stacked = jnp.stack([keys, values], axis=2).reshape(tok_grp, kv_heads * 2 * HEAD)
    cache_cols = 2 * KVH * HEAD // shards
    offset = tensor_rank * cache_cols - kv_first * 2 * HEAD
    own_cache = lax.dynamic_slice_in_dim(stacked, offset, cache_cols, 1)
    pages = own_cache.reshape(tok_grp // PAGE, PAGE, cache_cols)
    kv_pages = jnp.zeros_like(pages).at[page_table[0]].set(pages)
    share = q_heads // kv_heads
    grouped_q = queries.reshape(tok_grp, kv_heads, share, HEAD)
    scale = 1.0 / math.sqrt(HEAD)
    block = min(BLOCK_ROWS, tok_grp)
    outputs = []
    for first in range(0, tok_grp, block):
        last = first + block
        low = max(0, (first - LONGEST) // block * block)
        scores = (
            jnp.einsum(
                "ikgd,jkd->kgij",
                grouped_q[first:last],
                keys[low:last],
                preferred_element_type=jnp.float32,
            )
            * scale
        )
        query_rows = index[first:last]
        allowed = jnp.logical_and(
            query_rows[:, None] >= index[None, low:last],
            starts[first:last][:, None] <= index[None, low:last],
        )
        weights = jnp.where(allowed, jnp.exp(scores), 0.0)
        probs = (weights / jnp.sum(weights, axis=-1, keepdims=True)).astype(jnp.bfloat16)
        mixed = jnp.einsum(
            "kgij,jkd->ikgd", probs, values[low:last], preferred_element_type=jnp.float32
        )
        outputs.append(mixed.astype(jnp.bfloat16).reshape(block, q_heads * HEAD))
    attended = jnp.concatenate(outputs, axis=0)
    attended_full = lax.all_gather(attended, "tensor", axis=1, tiled=True)
    attn_sum = jnp.dot(attended_full, w_out_full, preferred_element_type=jnp.float32)
    middle = (full.astype(jnp.float32) + attn_sum).astype(jnp.bfloat16)
    ffn_in = rms_scale(middle, ffn_gain).astype(jnp.bfloat16)
    ff_part = w_gate.shape[1]
    gate_up = jnp.dot(
        ffn_in, jnp.concatenate([w_gate, w_up], axis=1), preferred_element_type=jnp.float32
    )
    gate = gate_up[:, :ff_part]
    upper = gate_up[:, ff_part:]
    hidden = (jax.nn.silu(gate) * upper).astype(jnp.bfloat16)
    ffn_part = lax.psum_scatter(
        jnp.dot(hidden, w_down, preferred_element_type=jnp.float32).astype(jnp.bfloat16),
        "tensor",
        scatter_dimension=1,
        tiled=True,
    ).astype(jnp.float32)
    own_cols = lax.dynamic_slice_in_dim(middle, tensor_rank * feat_part, feat_part, 1)
    combined = (own_cols.astype(jnp.float32) + ffn_part).astype(jnp.bfloat16)
    back = jnp.take(combined.reshape(units, unit_rows, feat_part), pos_of_slot, axis=0, mode="clip")
    returned = lax.all_to_all(
        back.reshape(groups, MOST, unit_rows, feat_part), "dp", split_axis=0, concat_axis=0, tiled=True
    ).reshape(slot_count, unit_rows, feat_part)
    result = jnp.take(returned, slot, axis=0, mode="clip")
    return (result.reshape(tok_grp, feat_part), kv_pages)


def solution(mesh):
    return jax.shard_map(
        on_device,
        mesh=mesh,
        in_specs=(
            P("dp", "tensor"),
            P("dp", None),
            P("dp", None),
            P("dp", None),
            P(),
            P(None, "tensor"),
            P(),
            P(),
            P(),
            P("tensor", None),
            P(),
            P(None, "tensor"),
            P(None, "tensor"),
            P("tensor", None),
        ),
        out_specs=(P("dp", "tensor"), P("dp", None, "tensor")),
        check_vma=False,
    )
```
